256 devices in a mesh: obs: 64 (over y, x, z_lo), ens: 4 (over z_hi, core).
Axes of the slice: x: 4, y: 4, z: 8 (z_hi: 2, z_lo: 4; z = z_hi * 4 + z_lo), core: 2. Of those that a mesh axis runs over, the one named last changes fastest.
Arguments:
- predicted: bfloat16 [262144, 512], P('obs', 'ens'), as said below
- noise: bfloat16 [262144, 512], P('obs', 'ens'), may hold values from -5 to 5
- observed: float32 [262144], P('obs'), as said below
- obs_error: float32 [262144], P('obs'), as said below
- coefficients: float32 [2000, 512], P('ens'), may hold values from -6 to 6
- basis: bfloat16 [2000, 262144], P(None, ('obs', 'ens')), may hold values from -0.125 to 0.125
- mean_field: float32 [262144], P(('obs', 'ens')), may hold values from -5 to 5
Outputs:
- updated: float32 [2000, 512], P('ens')
- field: bfloat16 [512, 262144], P(None, ('obs', 'ens'))
The draws below stay inside these ranges and needn't reach their ends.
Inputs may be any that keep to these rules, and one draw needn't show every extreme that they name: `observed`: observed data of order sqrt(512). `obs_error`: error deviations between half and twice sqrt(512). `predicted`: predicted data of order one.
All inputs are finite; a program needn't handle non-finite values.
Results may differ from the reference program's by a relative error of at most 0.0095.
Values may be sent and summed in bfloat16 or wider, within the bound.
No kernel may reach another device: no remote copies, remote signals or barrier semaphores. Data moves between devices by JAX's collectives and lax.ppermute only.
A program may use at most 64 MiB of HBM per device.

```python
import math
import jax
import jax.numpy as jnp
from jax import lax

MEMBERS = 512
LATENT = 2000
ALPHA = 4
OBS_DEV = 4096
NOBS = 262144
NCELL = 262144


def draw_observed(key, part):
    factor = 2.0 * math.sqrt(NOBS / MEMBERS)
    values = jnp.clip(jax.random.normal(key, (NOBS,), jnp.float32), -4.0, 4.0)
    return (values * factor).astype(jnp.float32)


def draw_obs_error(key, part):
    factor = math.sqrt(NOBS / MEMBERS)
    values = jnp.exp(jax.random.uniform(key, (NOBS,), jnp.float32, math.log(0.5), math.log(2.0)))
    return (values * factor).astype(jnp.float32)


def draw_predicted(key, part):
    mode_count = max(MEMBERS // 32, 4)
    load_reach = 128 // math.isqrt(mode_count)
    key_main = jax.random.fold_in(key, 11)
    key_load = jax.random.fold_in(key, 12)
    key_sign = jax.random.fold_in(key, 13)
    loadings = jax.random.randint(key_load, (NOBS, mode_count), -load_reach, load_reach + 1).astype(jnp.float32) / 64.0
    member_signs = (jax.random.randint(key_sign, (mode_count, MEMBERS), 0, 2) * 2 - 1).astype(jnp.float32)
    common = jnp.zeros((NOBS, MEMBERS), jnp.float32)
    for which_mode in range(mode_count):
        common = common + loadings[:, which_mode:which_mode + 1] * member_signs[which_mode:which_mode + 1, :]
    single = jnp.clip(jax.random.normal(key_main, (NOBS, MEMBERS), jnp.float32), -4.0, 4.0)
    return (single + common).astype(jnp.bfloat16)


def shard_levels(own_key, shape, split, low, top_value):
    factor_of, own = 1.0, jax.random.fold_in(own_key, 6)
    for position, parts in split:
        draws = jnp.exp(jax.random.uniform(jax.random.fold_in(own, position), (parts,), jnp.float32, low / len(split), top_value / len(split)))
        factor_of = factor_of * jnp.repeat(draws, shape[position] // parts).reshape([-1 if axis == position else 1 for axis in range(len(shape))])
    return factor_of


def bell_draw(rng, extent, deviation, limit, cuts=(), kind=jnp.bfloat16):
    entries = deviation * jax.random.normal(rng, extent, jnp.float32)
    if cuts:
        entries = entries * shard_levels(rng, extent, cuts, -0.22, 0.18)
    return jnp.clip(entries, -limit, limit).astype(kind)


def setup_inputs(seed: int = 0) -> dict:
    key_of = jax.random.split(jax.random.key(seed), 8)
    return {
        "predicted": draw_predicted(jax.random.fold_in(key_of[7], 71), 0),
        "noise": bell_draw(key_of[1], (NOBS, MEMBERS), 1.0, 5.0, ((0, 64), (1, 4))),
        "observed": draw_observed(jax.random.fold_in(key_of[7], 71), 0),
        "obs_error": draw_obs_error(jax.random.fold_in(key_of[7], 71), 0),
        "coefficients": bell_draw(key_of[4], (LATENT, MEMBERS), 1.0, 6.0, ((0, 4),), jnp.float32),
        "basis": bell_draw(key_of[5], (LATENT, NCELL), LATENT ** -0.5, 0.125, ((1, 256),)),
        "mean_field": bell_draw(key_of[6], (NCELL,), 1.0, 5.0, ((0, 256),), jnp.float32),
    }


def reference(predicted, noise, observed, obs_error, coefficients, basis, mean_field):
    spread = ALPHA ** 0.5 * obs_error
    block_count = NOBS // OBS_DEV

    def accumulate(carry, piece):
        gram_acc, cross_acc = carry
        pred_rows, noise_rows, obs_rows, spread_rows = piece
        pred_wide = pred_rows.astype(jnp.float32)
        innovation = ((obs_rows[:, None] - pred_wide) / spread_rows[:, None] + noise_rows.astype(jnp.float32)).astype(jnp.bfloat16)
        row_mean = jnp.mean(pred_wide, axis=1, keepdims=True)
        anomaly = ((pred_wide - row_mean) / ((MEMBERS - 1) ** 0.5 * spread_rows[:, None])).astype(jnp.bfloat16)
        gram_acc = gram_acc + jnp.dot(anomaly.T.astype(jnp.float32), anomaly.astype(jnp.float32), preferred_element_type=jnp.float32)
        cross_acc = cross_acc + jnp.dot(anomaly.T.astype(jnp.float32), innovation.astype(jnp.float32), preferred_element_type=jnp.float32)
        return ((gram_acc, cross_acc), None)
    pieces = (predicted.reshape(block_count, OBS_DEV, MEMBERS), noise.reshape(block_count, OBS_DEV, MEMBERS), observed.reshape(block_count, OBS_DEV), spread.reshape(block_count, OBS_DEV))
    initial = (jnp.zeros((MEMBERS, MEMBERS), jnp.float32), jnp.zeros((MEMBERS, MEMBERS), jnp.float32))
    (gram_sum, cross), _ = lax.scan(accumulate, initial, pieces)
    gram = gram_sum + jnp.eye(MEMBERS, dtype=jnp.float32)
    factor = jnp.linalg.cholesky(gram)
    weights = jax.scipy.linalg.cho_solve((factor, True), cross)
    coef_mean = jnp.mean(coefficients, axis=1, keepdims=True)
    coef_anomaly = (coefficients - coef_mean) / (MEMBERS - 1) ** 0.5
    updated = coefficients + jnp.dot(coef_anomaly, weights, precision=lax.Precision.HIGHEST)
    coef_low = updated.astype(jnp.bfloat16)
    rebuilt = jnp.dot(coef_low.T.astype(jnp.float32), basis.astype(jnp.float32), preferred_element_type=jnp.float32)
    field = (mean_field[None, :] + rebuilt).astype(jnp.bfloat16)
    return (updated, field)
```

```python
import jax
import jax.numpy as jnp
from jax import lax
from jax.sharding import Mesh
from jax.sharding import PartitionSpec as P

ALPHA = 4
OBS_AXES = ("y", "x", "zl")


def member_products(gathered, innov_all, row_scale, members):
    pred_wide = gathered.astype(jnp.float32)
    row_mean = jnp.mean(pred_wide, axis=1, keepdims=True)
    anomaly = ((pred_wide - row_mean) / ((members - 1) ** 0.5 * row_scale[:, None])).astype(
        jnp.bfloat16
    )
    contract = (((0,), (0,)), ((), ()))
    gram_part = lax.dot_general(anomaly, anomaly, contract, preferred_element_type=jnp.float32)
    cross_part = lax.dot_general(anomaly, innov_all, contract, preferred_element_type=jnp.float32)
    return (gram_part, cross_part)


def ring_psum(x, axes):
    for a in axes:
        n = lax.axis_size(a)
        idx = lax.axis_index(a)
        chunks = x.reshape(n, x.shape[0] // n, *x.shape[1:])
        acc = lax.dynamic_index_in_dim(chunks, idx, 0, keepdims=False)
        for s in range(1, n):
            send = lax.dynamic_index_in_dim(chunks, (idx + s) % n, 0, keepdims=False)
            acc = acc + lax.ppermute(send, a, [(i, (i + s) % n) for i in range(n)])
        x = acc
    for a in reversed(axes):
        n = lax.axis_size(a)
        idx = lax.axis_index(a)
        parts = [x] + [lax.ppermute(x, a, [(i, (i - s) % n) for i in range(n)]) for s in range(1, n)]
        x = jnp.roll(jnp.stack(parts), idx, axis=0).reshape(n * x.shape[0], *x.shape[1:])
    return x


def shards(predicted, noise, observed, obs_error, coefficients, basis, mean_field):
    row_count, group_size = predicted.shape
    members = group_size * lax.axis_size("ens")
    spread = ALPHA**0.5 * obs_error
    innovation = (
        (observed[:, None] - predicted.astype(jnp.float32)) / spread[:, None]
        + noise.astype(jnp.float32)
    ).astype(jnp.bfloat16)
    gathered, innov_all = (
        lax.all_gather(predicted, "ens", axis=1, tiled=True),
        lax.all_gather(innovation, "ens", axis=1, tiled=True),
    )
    gram_part, cross_part = member_products(gathered, innov_all, spread, members)
    both = ring_psum(jnp.concatenate([gram_part, cross_part], axis=0), OBS_AXES)
    gram_sum, cross = both[:members], both[members:]
    gram = gram_sum + jnp.eye(members, dtype=jnp.float32)
    factor = jnp.linalg.cholesky(gram)
    weights = jax.scipy.linalg.cho_solve((factor, True), cross)
    coef_mean = jnp.mean(coefficients, axis=1, keepdims=True)
    coef_anomaly = (coefficients - coef_mean) / (members - 1) ** 0.5
    updated = coefficients + jnp.dot(coef_anomaly, weights, precision=lax.Precision.HIGHEST)
    coef_low = updated.astype(jnp.bfloat16)
    rebuilt = lax.dot_general(
        lax.all_gather(coef_low, "ens", axis=0, tiled=True),
        basis,
        (((0,), (0,)), ((), ())),
        preferred_element_type=jnp.float32,
    )
    field = (mean_field[None, :] + rebuilt).astype(jnp.bfloat16)
    return (updated, field)


def solution(mesh):
    obs_size, ens_size = mesh.devices.shape
    side = round(obs_size ** (1 / 3))
    fine = Mesh(mesh.devices.reshape(side, side, obs_size // side**2, ens_size), (*OBS_AXES, "ens"))
    obs = OBS_AXES
    in_specs = (
        P(obs, "ens"),
        P(obs, "ens"),
        P(obs),
        P(obs),
        P("ens", None),
        P(None, (*obs, "ens")),
        P((*obs, "ens")),
    )
    out_specs = (P("ens", None), P(None, (*obs, "ens")))
    return jax.shard_map(shards, mesh=fine, in_specs=in_specs, out_specs=out_specs, check_vma=False)
```

```python
import jax
import jax.numpy as jnp
from jax import lax
from jax.sharding import Mesh
from jax.sharding import PartitionSpec as P

ALPHA = 4
OBS_AXES = ("y", "x", "zl")


def reduce_scatter(x, a):
    n = lax.axis_size(a)
    idx = lax.axis_index(a)
    chunks = x.reshape(n, x.shape[0] // n, *x.shape[1:])
    acc = lax.dynamic_index_in_dim(chunks, idx, 0, keepdims=False)
    for s in range(1, n):
        send = lax.dynamic_index_in_dim(chunks, (idx + s) % n, 0, keepdims=False)
        acc = acc + lax.ppermute(send, a, [(i, (i + s) % n) for i in range(n)])
    return acc


def gather(x, a):
    n = lax.axis_size(a)
    idx = lax.axis_index(a)
    parts = [x] + [lax.ppermute(x, a, [(i, (i - s) % n) for i in range(n)]) for s in range(1, n)]
    return jnp.roll(jnp.stack(parts), idx, axis=0)


def shards(predicted, noise, observed, obs_error, coefficients, basis, mean_field):
    row_count, group_size = predicted.shape
    ens_size = lax.axis_size("ens")
    members = group_size * ens_size
    spread = ALPHA**0.5 * obs_error
    innovation = (
        (observed[:, None] - predicted.astype(jnp.float32)) / spread[:, None]
        + noise.astype(jnp.float32)
    ).astype(jnp.bfloat16)
    coef_all = lax.all_gather(coefficients, "ens", axis=0, tiled=True)
    pred_wide = lax.all_gather(predicted, "ens", axis=1, tiled=True).astype(jnp.float32)
    row_mean = jnp.mean(pred_wide, axis=1, keepdims=True)
    anomaly = ((pred_wide - row_mean) / ((members - 1) ** 0.5 * spread[:, None])).astype(jnp.bfloat16)
    own = lax.dynamic_slice_in_dim(anomaly, lax.axis_index("ens") * group_size, group_size, axis=1)
    contract = (((0,), (0,)), ((), ()))
    gram_part = lax.dot_general(anomaly, own, contract, preferred_element_type=jnp.float32)
    cross_part = lax.dot_general(anomaly, innovation, contract, preferred_element_type=jnp.float32)
    x = jnp.concatenate([gram_part, cross_part], axis=0)
    for a in OBS_AXES:
        x = reduce_scatter(x, a)
    x = gather(x, "ens")
    for a in reversed(OBS_AXES):
        x = gather(x, a)
    x = jnp.moveaxis(x, 3, 4).reshape(2 * members, members)
    gram_sum, cross = x[:members], x[members:]
    gram = gram_sum + jnp.eye(members, dtype=jnp.float32)
    factor = jnp.linalg.cholesky(gram)
    weights = jax.scipy.linalg.cho_solve((factor, True), cross)
    coef_mean = jnp.mean(coef_all, axis=1, keepdims=True)
    coef_anomaly = (coef_all - coef_mean) / (members - 1) ** 0.5
    updated_all = coef_all + jnp.dot(coef_anomaly, weights, precision=lax.Precision.HIGHEST)
    coef_low = updated_all.astype(jnp.bfloat16)
    rebuilt = lax.dot_general(
        coef_low, basis, (((0,), (0,)), ((), ())), preferred_element_type=jnp.float32
    )
    field = (mean_field[None, :] + rebuilt).astype(jnp.bfloat16)
    rows = coefficients.shape[0]
    updated = lax.dynamic_slice_in_dim(updated_all, lax.axis_index("ens") * rows, rows, axis=0)
    return (updated, field)


def solution(mesh):
    obs_size, ens_size = mesh.devices.shape
    side = round(obs_size ** (1 / 3))
    fine = Mesh(mesh.devices.reshape(side, side, obs_size // side**2, ens_size), (*OBS_AXES, "ens"))
    obs = OBS_AXES
    in_specs = (
        P(obs, "ens"),
        P(obs, "ens"),
        P(obs),
        P(obs),
        P("ens", None),
        P(None, (*obs, "ens")),
        P((*obs, "ens")),
    )
    out_specs = (P("ens", None), P(None, (*obs, "ens")))
    return jax.shard_map(shards, mesh=fine, in_specs=in_specs, out_specs=out_specs, check_vma=False)
```

```python
import jax
import jax.numpy as jnp
from jax import lax
from jax.sharding import Mesh
from jax.sharding import PartitionSpec as P

ALPHA = 4
OBS_AXES = ("y", "x", "zl")


def reduce_scatter(x, a):
    n = lax.axis_size(a)
    idx = lax.axis_index(a)
    chunks = x.reshape(n, x.shape[0] // n, *x.shape[1:])
    acc = lax.dynamic_index_in_dim(chunks, idx, 0, keepdims=False)
    for s in range(1, n):
        send = lax.dynamic_index_in_dim(chunks, (idx + s) % n, 0, keepdims=False)
        acc = acc + lax.ppermute(send, a, [(i, (i + s) % n) for i in range(n)])
    return acc


def gather(x, a):
    n = lax.axis_size(a)
    idx = lax.axis_index(a)
    parts = [x] + [lax.ppermute(x, a, [(i, (i - s) % n) for i in range(n)]) for s in range(1, n)]
    return jnp.roll(jnp.stack(parts), idx, axis=0)


def dot(a, b):
    return jnp.dot(a, b, precision=lax.Precision.HIGHEST)


def factor_inverse(m, base=128):
    n = m.shape[0]
    if n <= base:
        low = jnp.linalg.cholesky(m)
        return jax.scipy.linalg.solve_triangular(low, jnp.eye(n, dtype=m.dtype), lower=True)
    h = n // 2
    top_inv = factor_inverse(m[:h, :h], base)
    left = dot(m[h:, :h], top_inv.T)
    bottom_inv = factor_inverse(m[h:, h:] - dot(left, left.T), base)
    corner = -dot(bottom_inv, dot(left, top_inv))
    upper = jnp.concatenate([top_inv, jnp.zeros((h, n - h), m.dtype)], axis=1)
    lower = jnp.concatenate([corner, bottom_inv], axis=1)
    return jnp.concatenate([upper, lower], axis=0)


def shards(predicted, noise, observed, obs_error, coefficients, basis, mean_field):
    row_count, group_size = predicted.shape
    ens_size = lax.axis_size("ens")
    members = group_size * ens_size
    spread = ALPHA**0.5 * obs_error
    innovation = (
        (observed[:, None] - predicted.astype(jnp.float32)) / spread[:, None]
        + noise.astype(jnp.float32)
    ).astype(jnp.bfloat16)
    coef_all = lax.all_gather(coefficients, "ens", axis=0, tiled=True)
    e = lax.axis_index("ens")
    two = jnp.stack([predicted, lax.ppermute(predicted, "ens", [(i, i ^ 2) for i in range(ens_size)])])
    four = jnp.concatenate([two, lax.ppermute(two, "ens", [(i, i ^ 1) for i in range(ens_size)])])
    blocks = jnp.take(four, jnp.array([0, 2, 1, 3])[jnp.arange(ens_size) ^ e], axis=0).astype(jnp.float32)
    row_mean = jnp.sum(blocks, axis=(0, 2)) / members
    anomaly = ((blocks - row_mean[None, :, None]) / ((members - 1) ** 0.5 * spread[None, :, None])).astype(
        jnp.bfloat16
    )
    own = lax.dynamic_index_in_dim(anomaly, e, 0, keepdims=False)
    contract = (((1,), (0,)), ((), ()))
    gram_part = lax.dot_general(anomaly, own, contract, preferred_element_type=jnp.float32).reshape(members, -1)
    cross_part = lax.dot_general(anomaly, innovation, contract, preferred_element_type=jnp.float32).reshape(
        members, -1
    )
    x = jnp.concatenate([gram_part, cross_part], axis=0)
    for a in OBS_AXES:
        x = reduce_scatter(x, a)
    x = gather(x, "ens")
    for a in reversed(OBS_AXES):
        x = gather(x, a)
    x = jnp.moveaxis(x, 3, 4).reshape(2 * members, members)
    gram_sum, cross = x[:members], x[members:]
    gram = gram_sum + jnp.eye(members, dtype=jnp.float32)
    factor_inv = factor_inverse(gram)
    weights = dot(factor_inv.T, dot(factor_inv, cross))
    coef_mean = jnp.mean(coef_all, axis=1, keepdims=True)
    coef_anomaly = (coef_all - coef_mean) / (members - 1) ** 0.5
    updated_all = coef_all + jnp.dot(coef_anomaly, weights, precision=lax.Precision.HIGHEST)
    coef_low = updated_all.astype(jnp.bfloat16)
    rebuilt = lax.dot_general(
        coef_low, basis, (((0,), (0,)), ((), ())), preferred_element_type=jnp.float32
    )
    field = (mean_field[None, :] + rebuilt).astype(jnp.bfloat16)
    rows = coefficients.shape[0]
    updated = lax.dynamic_slice_in_dim(updated_all, lax.axis_index("ens") * rows, rows, axis=0)
    return (updated, field)


def solution(mesh):
    obs_size, ens_size = mesh.devices.shape
    side = round(obs_size ** (1 / 3))
    fine = Mesh(mesh.devices.reshape(side, side, obs_size // side**2, ens_size), (*OBS_AXES, "ens"))
    obs = OBS_AXES
    in_specs = (
        P(obs, "ens"),
        P(obs, "ens"),
        P(obs),
        P(obs),
        P("ens", None),
        P(None, (*obs, "ens")),
        P((*obs, "ens")),
    )
    out_specs = (P("ens", None), P(None, (*obs, "ens")))
    return jax.shard_map(shards, mesh=fine, in_specs=in_specs, out_specs=out_specs, check_vma=False)
```

```python
import jax
import jax.numpy as jnp
from jax import lax
from jax.sharding import Mesh
from jax.sharding import PartitionSpec as P

ALPHA = 4
OBS_AXES = ("y", "x", "zl")


def reduce_scatter(x, a):
    n = lax.axis_size(a)
    idx = lax.axis_index(a)
    chunks = x.reshape(n, x.shape[0] // n, *x.shape[1:])
    acc = lax.dynamic_index_in_dim(chunks, idx, 0, keepdims=False)
    for s in range(1, n):
        send = lax.dynamic_index_in_dim(chunks, (idx + s) % n, 0, keepdims=False)
        acc = acc + lax.ppermute(send, a, [(i, (i + s) % n) for i in range(n)])
    return acc


def gather(x, a):
    n = lax.axis_size(a)
    idx = lax.axis_index(a)
    parts = [x] + [lax.ppermute(x, a, [(i, (i - s) % n) for i in range(n)]) for s in range(1, n)]
    return jnp.roll(jnp.stack(parts), idx, axis=0)


def dot(a, b):
    return jnp.dot(a, b, precision=lax.Precision.HIGHEST)


def factor_inverse(m, base=128):
    n = m.shape[0]
    if n <= base:
        low = jnp.linalg.cholesky(m)
        return jax.scipy.linalg.solve_triangular(low, jnp.eye(n, dtype=m.dtype), lower=True)
    h = n // 2
    top_inv = factor_inverse(m[:h, :h], base)
    left = dot(m[h:, :h], top_inv.T)
    bottom_inv = factor_inverse(m[h:, h:] - dot(left, left.T), base)
    corner = -dot(bottom_inv, dot(left, top_inv))
    upper = jnp.concatenate([top_inv, jnp.zeros((h, n - h), m.dtype)], axis=1)
    lower = jnp.concatenate([corner, bottom_inv], axis=1)
    return jnp.concatenate([upper, lower], axis=0)


def shards(predicted, noise, observed, obs_error, coefficients, basis, mean_field):
    row_count, group_size = predicted.shape
    ens_size = lax.axis_size("ens")
    members = group_size * ens_size
    spread = ALPHA**0.5 * obs_error
    innovation = (
        (observed[:, None] - predicted.astype(jnp.float32)) / spread[:, None]
        + noise.astype(jnp.float32)
    ).astype(jnp.bfloat16)
    coef_all = lax.all_gather(coefficients, "ens", axis=0, tiled=True)
    e = lax.axis_index("ens")
    partner = lax.ppermute(predicted, "ens", [(i, i ^ 2) for i in range(ens_size)])
    other = lax.ppermute(jnp.stack([predicted, partner]), "ens", [(i, i ^ 1) for i in range(ens_size)])
    pieces = [(0, predicted), (2, partner), (1, other[0]), (3, other[1])]
    wide = [p.astype(jnp.float32) for _, p in pieces]
    row_mean = (wide[0] + wide[1] + wide[2] + wide[3]).sum(axis=1) / members
    scale = (members - 1) ** 0.5 * spread[:, None]
    anomaly = [((w - row_mean[:, None]) / scale).astype(jnp.bfloat16) for w in wide]
    lead = jnp.concatenate([anomaly[0], innovation], axis=1)
    contract = (((0,), (0,)), ((), ()))
    x = jnp.zeros((2 * group_size, members), jnp.float32)
    for (flip, _), a in zip(pieces, anomaly):
        part = lax.dot_general(lead, a, contract, preferred_element_type=jnp.float32)
        x = lax.dynamic_update_slice_in_dim(x, part, (e ^ flip) * group_size, axis=1)
    for a in OBS_AXES:
        x = reduce_scatter(x, a)
    x = gather(x, "ens")
    for a in reversed(OBS_AXES):
        x = gather(x, a)
    x = jnp.moveaxis(x, 3, 0).reshape(ens_size, 2, group_size, members)
    gram_sum = x[:, 0].reshape(members, members)
    cross = x[:, 1].reshape(members, members).T
    gram = gram_sum + jnp.eye(members, dtype=jnp.float32)
    factor_inv = factor_inverse(gram)
    weights = dot(factor_inv.T, dot(factor_inv, cross))
    coef_mean = jnp.mean(coef_all, axis=1, keepdims=True)
    coef_anomaly = (coef_all - coef_mean) / (members - 1) ** 0.5
    updated_all = coef_all + jnp.dot(coef_anomaly, weights, precision=lax.Precision.HIGH)
    coef_low = updated_all.astype(jnp.bfloat16)
    rebuilt = lax.dot_general(
        coef_low, basis, (((0,), (0,)), ((), ())), preferred_element_type=jnp.float32
    )
    field = (mean_field[None, :] + rebuilt).astype(jnp.bfloat16)
    rows = coefficients.shape[0]
    updated = lax.dynamic_slice_in_dim(updated_all, lax.axis_index("ens") * rows, rows, axis=0)
    return (updated, field)


def solution(mesh):
    obs_size, ens_size = mesh.devices.shape
    side = round(obs_size ** (1 / 3))
    fine = Mesh(mesh.devices.reshape(side, side, obs_size // side**2, ens_size), (*OBS_AXES, "ens"))
    obs = OBS_AXES
    in_specs = (
        P(obs, "ens"),
        P(obs, "ens"),
        P(obs),
        P(obs),
        P("ens", None),
        P(None, (*obs, "ens")),
        P((*obs, "ens")),
    )
    out_specs = (P("ens", None), P(None, (*obs, "ens")))
    return jax.shard_map(shards, mesh=fine, in_specs=in_specs, out_specs=out_specs, check_vma=False)
```

```python
import jax
import jax.numpy as jnp
from jax import lax
from jax.sharding import Mesh
from jax.sharding import PartitionSpec as P

ALPHA = 4
OBS_AXES = ("y", "x", "zl")


def reduce_scatter(x, a):
    n = lax.axis_size(a)
    idx = lax.axis_index(a)
    chunks = x.reshape(n, x.shape[0] // n, *x.shape[1:])
    acc = lax.dynamic_index_in_dim(chunks, idx, 0, keepdims=False)
    for s in range(1, n):
        send = lax.dynamic_index_in_dim(chunks, (idx + s) % n, 0, keepdims=False)
        acc = acc + lax.ppermute(send, a, [(i, (i + s) % n) for i in range(n)])
    return acc


def gather(x, a):
    n = lax.axis_size(a)
    idx = lax.axis_index(a)
    parts = [x] + [lax.ppermute(x, a, [(i, (i - s) % n) for i in range(n)]) for s in range(1, n)]
    return jnp.roll(jnp.stack(parts), idx, axis=0)


def dot(a, b):
    return jnp.dot(a, b, precision=lax.Precision.HIGHEST)


def factor_inverse(m, base=128):
    n = m.shape[0]
    if n <= base:
        low = jnp.linalg.cholesky(m)
        return jax.scipy.linalg.solve_triangular(low, jnp.eye(n, dtype=m.dtype), lower=True)
    h = n // 2
    top_inv = factor_inverse(m[:h, :h], base)
    left = dot(m[h:, :h], top_inv.T)
    bottom_inv = factor_inverse(m[h:, h:] - dot(left, left.T), base)
    corner = -dot(bottom_inv, dot(left, top_inv))
    upper = jnp.concatenate([top_inv, jnp.zeros((h, n - h), m.dtype)], axis=1)
    lower = jnp.concatenate([corner, bottom_inv], axis=1)
    return jnp.concatenate([upper, lower], axis=0)


def shards(predicted, noise, observed, obs_error, coefficients, basis, mean_field):
    row_count, group_size = predicted.shape
    ens_size = lax.axis_size("ens")
    members = group_size * ens_size
    spread = ALPHA**0.5 * obs_error
    innovation = (
        (observed[:, None] - predicted.astype(jnp.float32)) / spread[:, None]
        + noise.astype(jnp.float32)
    ).astype(jnp.bfloat16)
    coef_all = lax.all_gather(coefficients, "ens", axis=0, tiled=True)
    e = lax.axis_index("ens")
    partner = lax.ppermute(predicted, "ens", [(i, i ^ 2) for i in range(ens_size)])
    other = lax.ppermute(jnp.stack([predicted, partner]), "ens", [(i, i ^ 1) for i in range(ens_size)])
    pieces = [(0, predicted), (2, partner), (1, other[0]), (3, other[1])]
    wide = [p.astype(jnp.float32) for _, p in pieces]
    row_mean = (wide[0] + wide[1] + wide[2] + wide[3]).sum(axis=1) / members
    scale = (members - 1) ** 0.5 * spread[:, None]
    anomaly = [((w - row_mean[:, None]) / scale).astype(jnp.bfloat16) for w in wide]
    lead = jnp.concatenate([anomaly[0], innovation], axis=1)
    contract = (((0,), (0,)), ((), ()))
    x = jnp.zeros((2 * group_size, members), jnp.float32)
    for (flip, _), a in zip(pieces, anomaly):
        part = lax.dot_general(lead, a, contract, preferred_element_type=jnp.float32)
        x = lax.dynamic_update_slice_in_dim(x, part, (e ^ flip) * group_size, axis=1)
    x = reduce_scatter(reduce_scatter(x, "y"), "x")
    parts = gather(x, "zl")
    x = ((parts[0] + parts[1]) + parts[2]) + parts[3]
    x = gather(gather(gather(x, "ens"), "x"), "y")
    x = jnp.moveaxis(x, 2, 0).reshape(ens_size, 2, group_size, members)
    gram_sum = x[:, 0].reshape(members, members)
    cross = x[:, 1].reshape(members, members).T
    gram = gram_sum + jnp.eye(members, dtype=jnp.float32)
    factor_inv = factor_inverse(gram)
    weights = dot(factor_inv.T, dot(factor_inv, cross))
    coef_mean = jnp.mean(coef_all, axis=1, keepdims=True)
    coef_anomaly = (coef_all - coef_mean) / (members - 1) ** 0.5
    updated_all = coef_all + jnp.dot(coef_anomaly, weights, precision=lax.Precision.HIGH)
    coef_low = updated_all.astype(jnp.bfloat16)
    rebuilt = lax.dot_general(
        coef_low, basis, (((0,), (0,)), ((), ())), preferred_element_type=jnp.float32
    )
    field = (mean_field[None, :] + rebuilt).astype(jnp.bfloat16)
    rows = coefficients.shape[0]
    updated = lax.dynamic_slice_in_dim(updated_all, lax.axis_index("ens") * rows, rows, axis=0)
    return (updated, field)


def solution(mesh):
    obs_size, ens_size = mesh.devices.shape
    side = round(obs_size ** (1 / 3))
    fine = Mesh(mesh.devices.reshape(side, side, obs_size // side**2, ens_size), (*OBS_AXES, "ens"))
    obs = OBS_AXES
    in_specs = (
        P(obs, "ens"),
        P(obs, "ens"),
        P(obs),
        P(obs),
        P("ens", None),
        P(None, (*obs, "ens")),
        P((*obs, "ens")),
    )
    out_specs = (P("ens", None), P(None, (*obs, "ens")))
    return jax.shard_map(shards, mesh=fine, in_specs=in_specs, out_specs=out_specs, check_vma=False)
```

```python
import jax
import jax.numpy as jnp
from jax import lax
from jax.sharding import Mesh
from jax.sharding import PartitionSpec as P

ALPHA = 4
OBS_AXES = ("y", "x", "zl")


def reduce_scatter(x, a):
    n = lax.axis_size(a)
    idx = lax.axis_index(a)
    chunks = x.reshape(n, x.shape[0] // n, *x.shape[1:])
    acc = lax.dynamic_index_in_dim(chunks, idx, 0, keepdims=False)
    for s in range(1, n):
        send = lax.dynamic_index_in_dim(chunks, (idx + s) % n, 0, keepdims=False)
        acc = acc + lax.ppermute(send, a, [(i, (i + s) % n) for i in range(n)])
    return acc


def gather(x, a):
    n = lax.axis_size(a)
    idx = lax.axis_index(a)
    parts = [x] + [lax.ppermute(x, a, [(i, (i - s) % n) for i in range(n)]) for s in range(1, n)]
    return jnp.roll(jnp.stack(parts), idx, axis=0)


def dot(a, b):
    return jnp.dot(a, b, precision=lax.Precision.HIGHEST)


def factor_inverse(m, base=128):
    n = m.shape[0]
    if n <= base:
        low = jnp.linalg.cholesky(m)
        return jax.scipy.linalg.solve_triangular(low, jnp.eye(n, dtype=m.dtype), lower=True)
    h = n // 2
    top_inv = factor_inverse(m[:h, :h], base)
    left = dot(m[h:, :h], top_inv.T)
    bottom_inv = factor_inverse(m[h:, h:] - dot(left, left.T), base)
    corner = -dot(bottom_inv, dot(left, top_inv))
    upper = jnp.concatenate([top_inv, jnp.zeros((h, n - h), m.dtype)], axis=1)
    lower = jnp.concatenate([corner, bottom_inv], axis=1)
    return jnp.concatenate([upper, lower], axis=0)


def shards(predicted, noise, observed, obs_error, coefficients, basis, mean_field):
    row_count, group_size = predicted.shape
    ens_size = lax.axis_size("ens")
    members = group_size * ens_size
    spread = ALPHA**0.5 * obs_error
    innovation = (
        (observed[:, None] - predicted.astype(jnp.float32)) / spread[:, None]
        + noise.astype(jnp.float32)
    ).astype(jnp.bfloat16)
    e = lax.axis_index("ens")
    partner = lax.ppermute(predicted, "ens", [(i, i ^ 2) for i in range(ens_size)])
    coef_own, partner = lax.optimization_barrier((coefficients, partner))
    coef_partner = lax.ppermute(coef_own, "ens", [(i, i ^ 2) for i in range(ens_size)])
    coef_core = lax.ppermute(coefficients, "ens", [(i, i ^ 1) for i in range(ens_size)])
    other = lax.ppermute(jnp.stack([predicted, partner]), "ens", [(i, i ^ 1) for i in range(ens_size)])
    pieces = [(0, predicted), (2, partner), (1, other[0]), (3, other[1])]
    wide = [p.astype(jnp.float32) for _, p in pieces]
    row_mean = (wide[0] + wide[1] + wide[2] + wide[3]).sum(axis=1) / members
    scale = (members - 1) ** 0.5 * spread[:, None]
    anomaly = [((w - row_mean[:, None]) / scale).astype(jnp.bfloat16) for w in wide]
    lead = jnp.concatenate([anomaly[0], innovation], axis=1)
    contract = (((0,), (0,)), ((), ()))
    x = jnp.zeros((2 * group_size, members), jnp.float32)
    for (flip, _), a in zip(pieces, anomaly):
        part = lax.dot_general(lead, a, contract, preferred_element_type=jnp.float32)
        x = lax.dynamic_update_slice_in_dim(x, part, (e ^ flip) * group_size, axis=1)
    x = reduce_scatter(reduce_scatter(x, "y"), "x")
    parts = gather(x, "zl")
    x = ((parts[0] + parts[1]) + parts[2]) + parts[3]
    x = gather(gather(gather(x, "ens"), "x"), "y")
    x = jnp.moveaxis(x, 2, 0).reshape(ens_size, 2, group_size, members)
    gram_sum = x[:, 0].reshape(members, members)
    cross = x[:, 1].reshape(members, members).T
    gram = gram_sum + jnp.eye(members, dtype=jnp.float32)
    factor_inv = factor_inverse(gram)
    coef_partner, factor_inv = lax.optimization_barrier((coef_partner, factor_inv))
    weights = dot(factor_inv.T, dot(factor_inv, cross))
    coef_far = lax.ppermute(coef_partner, "ens", [(i, i ^ 1) for i in range(ens_size)])
    coef_blocks = jnp.stack([coef_own, coef_partner, coef_core, coef_far])
    coef_mean = jnp.mean(coef_blocks, axis=2, keepdims=True)
    coef_anomaly = (coef_blocks - coef_mean) / (members - 1) ** 0.5
    updated_blocks = coef_blocks + jnp.einsum(
        "krm,mn->krn", coef_anomaly, weights, precision=lax.Precision.HIGH
    )
    coef_low = jnp.take(
        updated_blocks.astype(jnp.bfloat16), jnp.array([0, 2, 1, 3])[jnp.arange(ens_size) ^ e], axis=0
    ).reshape(-1, members)
    rebuilt = lax.dot_general(
        coef_low, basis, (((0,), (0,)), ((), ())), preferred_element_type=jnp.float32
    )
    field = (mean_field[None, :] + rebuilt).astype(jnp.bfloat16)
    updated = updated_blocks[0]
    return (updated, field)


def solution(mesh):
    obs_size, ens_size = mesh.devices.shape
    side = round(obs_size ** (1 / 3))
    fine = Mesh(mesh.devices.reshape(side, side, obs_size // side**2, ens_size), (*OBS_AXES, "ens"))
    obs = OBS_AXES
    in_specs = (
        P(obs, "ens"),
        P(obs, "ens"),
        P(obs),
        P(obs),
        P("ens", None),
        P(None, (*obs, "ens")),
        P((*obs, "ens")),
    )
    out_specs = (P("ens", None), P(None, (*obs, "ens")))
    return jax.shard_map(shards, mesh=fine, in_specs=in_specs, out_specs=out_specs, check_vma=False)
```

```python
import jax
import jax.numpy as jnp
from jax import lax
from jax.sharding import Mesh
from jax.sharding import PartitionSpec as P


ALPHA = 4
OBS_AXES = ("y", "x", "zl")


def reduce_scatter(x, a):
    n = lax.axis_size(a)
    idx = lax.axis_index(a)
    chunks = x.reshape(n, x.shape[0] // n, *x.shape[1:])
    acc = lax.dynamic_index_in_dim(chunks, idx, 0, keepdims=False)
    for s in range(1, n):
        send = lax.dynamic_index_in_dim(chunks, (idx + s) % n, 0, keepdims=False)
        acc = acc + lax.ppermute(send, a, [(i, (i + s) % n) for i in range(n)])
    return acc


def gather(x, a):
    n = lax.axis_size(a)
    idx = lax.axis_index(a)
    parts = [x] + [lax.ppermute(x, a, [(i, (i - s) % n) for i in range(n)]) for s in range(1, n)]
    return jnp.roll(jnp.stack(parts), idx, axis=0)


def dot(a, b):
    return jnp.dot(a, b, precision=lax.Precision.HIGH)


def factor_inverse(m, base=128):
    n = m.shape[0]
    if n <= base:
        low = jnp.linalg.cholesky(m)
        return jax.scipy.linalg.solve_triangular(low, jnp.eye(n, dtype=m.dtype), lower=True)
    h = n // 2
    top_inv = factor_inverse(m[:h, :h], base)
    left = dot(m[h:, :h], top_inv.T)
    bottom_inv = factor_inverse(m[h:, h:] - dot(left, left.T), base)
    corner = -dot(bottom_inv, dot(left, top_inv))
    upper = jnp.concatenate([top_inv, jnp.zeros((h, n - h), m.dtype)], axis=1)
    lower = jnp.concatenate([corner, bottom_inv], axis=1)
    return jnp.concatenate([upper, lower], axis=0)


def shards(predicted, noise, observed, obs_error, coefficients, basis, mean_field):
    _, group_size = predicted.shape
    ens_size = lax.axis_size("ens")
    members = group_size * ens_size
    spread = ALPHA**0.5 * obs_error
    innovation = (
        (observed[:, None] - predicted.astype(jnp.float32)) / spread[:, None]
        + noise.astype(jnp.float32)
    ).astype(jnp.bfloat16)
    row_sum = predicted.astype(jnp.float32).sum(axis=1)
    row_sum = row_sum + lax.ppermute(row_sum, "ens", [(i, i ^ 2) for i in range(ens_size)])
    row_sum = row_sum + lax.ppermute(row_sum, "ens", [(i, i ^ 1) for i in range(ens_size)])
    row_mean = row_sum / members
    e = lax.axis_index("ens")
    core = lax.ppermute(predicted, "ens", [(i, i ^ 1) for i in range(ens_size)])
    partner = lax.ppermute(predicted, "ens", [(i, i ^ 2) for i in range(ens_size)])
    coef_own, partner = lax.optimization_barrier((coefficients, partner))
    coef_partner = lax.ppermute(coef_own, "ens", [(i, i ^ 2) for i in range(ens_size)])
    coef_core = lax.ppermute(coefficients, "ens", [(i, i ^ 1) for i in range(ens_size)])
    far = lax.ppermute(partner, "ens", [(i, i ^ 1) for i in range(ens_size)])
    pieces = [(0, predicted), (1, core), (2, partner), (3, far)]
    scale = (members - 1) ** 0.5 * spread[:, None]
    contract = (((0,), (0,)), ((), ()))
    x = jnp.zeros((2 * group_size, members), jnp.float32)
    lead = None
    for (flip, p) in pieces:
        a = ((p.astype(jnp.float32) - row_mean[:, None]) / scale).astype(jnp.bfloat16)
        if lead is None:
            lead = jnp.concatenate([a, innovation], axis=1)
        part = lax.dot_general(lead, a, contract, preferred_element_type=jnp.float32)
        x = lax.dynamic_update_slice_in_dim(x, part, (e ^ flip) * group_size, axis=1)
    x = reduce_scatter(reduce_scatter(x, "y"), "x")
    parts = gather(x, "zl")
    x = ((parts[0] + parts[1]) + parts[2]) + parts[3]
    x = gather(gather(gather(x, "ens"), "x"), "y")
    x = jnp.moveaxis(x, 2, 0).reshape(ens_size, 2, group_size, members)
    gram_sum = x[:, 0].reshape(members, members)
    cross = x[:, 1].reshape(members, members).T
    gram = gram_sum + jnp.eye(members, dtype=jnp.float32)
    factor_inv = factor_inverse(gram)
    coef_partner, factor_inv = lax.optimization_barrier((coef_partner, factor_inv))
    weights = dot(factor_inv.T, dot(factor_inv, cross))
    coef_far = lax.ppermute(coef_partner, "ens", [(i, i ^ 1) for i in range(ens_size)])
    coef_blocks = jnp.stack([coef_own, coef_partner, coef_core, coef_far])
    coef_mean = jnp.mean(coef_blocks, axis=2, keepdims=True)
    coef_anomaly = (coef_blocks - coef_mean) / (members - 1) ** 0.5
    updated_blocks = coef_blocks + jnp.einsum(
        "krm,mn->krn", coef_anomaly, weights, precision=lax.Precision.HIGH
    )
    coef_low = jnp.take(
        updated_blocks.astype(jnp.bfloat16), jnp.array([0, 2, 1, 3])[jnp.arange(ens_size) ^ e], axis=0
    ).reshape(-1, members)
    rebuilt = lax.dot_general(
        coef_low, basis, (((0,), (0,)), ((), ())), preferred_element_type=jnp.float32
    )
    field = (mean_field[None, :] + rebuilt).astype(jnp.bfloat16)
    updated = updated_blocks[0]
    return (updated, field)


def solution(mesh):
    obs_size, ens_size = mesh.devices.shape
    side = round(obs_size ** (1 / 3))
    fine = Mesh(mesh.devices.reshape(side, side, obs_size // side**2, ens_size), (*OBS_AXES, "ens"))
    obs = OBS_AXES
    in_specs = (
        P(obs, "ens"),
        P(obs, "ens"),
        P(obs),
        P(obs),
        P("ens", None),
        P(None, (*obs, "ens")),
        P((*obs, "ens")),
    )
    out_specs = (P("ens", None), P(None, (*obs, "ens")))
    return jax.shard_map(shards, mesh=fine, in_specs=in_specs, out_specs=out_specs, check_vma=False)
```

```python
import jax
import jax.numpy as jnp
from jax import lax
from jax.sharding import Mesh
from jax.sharding import PartitionSpec as P


ALPHA = 4
OBS_AXES = ("y", "x", "zl")


def reduce_scatter(x, a):
    n = lax.axis_size(a)
    idx = lax.axis_index(a)
    chunks = x.reshape(n, x.shape[0] // n, *x.shape[1:])
    acc = lax.dynamic_index_in_dim(chunks, idx, 0, keepdims=False)
    for s in range(1, n):
        send = lax.dynamic_index_in_dim(chunks, (idx + s) % n, 0, keepdims=False)
        acc = acc + lax.ppermute(send, a, [(i, (i + s) % n) for i in range(n)])
    return acc


def gather(x, a):
    n = lax.axis_size(a)
    idx = lax.axis_index(a)
    parts = [x] + [lax.ppermute(x, a, [(i, (i - s) % n) for i in range(n)]) for s in range(1, n)]
    return jnp.roll(jnp.stack(parts), idx, axis=0)


def dot(a, b):
    return jnp.dot(a, b, precision=lax.Precision.HIGH)


def factor_inverse(m, base=128):
    n = m.shape[0]
    if n <= base:
        low = jnp.linalg.cholesky(m)
        return jax.scipy.linalg.solve_triangular(low, jnp.eye(n, dtype=m.dtype), lower=True)
    h = n // 2
    top_inv = factor_inverse(m[:h, :h], base)
    left = dot(m[h:, :h], top_inv.T)
    bottom_inv = factor_inverse(m[h:, h:] - dot(left, left.T), base)
    corner = -dot(bottom_inv, dot(left, top_inv))
    upper = jnp.concatenate([top_inv, jnp.zeros((h, n - h), m.dtype)], axis=1)
    lower = jnp.concatenate([corner, bottom_inv], axis=1)
    return jnp.concatenate([upper, lower], axis=0)


def shards(predicted, noise, observed, obs_error, coefficients, basis, mean_field):
    _, group_size = predicted.shape
    ens_size = lax.axis_size("ens")
    members = group_size * ens_size
    spread = ALPHA**0.5 * obs_error
    innovation = (
        (observed[:, None] - predicted.astype(jnp.float32)) / spread[:, None]
        + noise.astype(jnp.float32)
    ).astype(jnp.bfloat16)
    row_sum = predicted.astype(jnp.float32).sum(axis=1)
    row_sum = row_sum + lax.ppermute(row_sum, "ens", [(i, i ^ 2) for i in range(ens_size)])
    row_sum = row_sum + lax.ppermute(row_sum, "ens", [(i, i ^ 1) for i in range(ens_size)])
    row_mean = row_sum / members
    e = lax.axis_index("ens")
    core = lax.ppermute(predicted, "ens", [(i, i ^ 1) for i in range(ens_size)])
    partner = lax.ppermute(predicted, "ens", [(i, i ^ 2) for i in range(ens_size)])
    coef_own, partner = lax.optimization_barrier((coefficients, partner))
    coef_partner = lax.ppermute(coef_own, "ens", [(i, i ^ 2) for i in range(ens_size)])
    coef_core = lax.ppermute(coefficients, "ens", [(i, i ^ 1) for i in range(ens_size)])
    far = lax.ppermute(partner, "ens", [(i, i ^ 1) for i in range(ens_size)])
    pieces = [(0, predicted), (1, core), (2, partner), (3, far)]
    scale = (members - 1) ** 0.5 * spread[:, None]
    contract = (((0,), (0,)), ((), ()))
    x = jnp.zeros((2 * group_size, members), jnp.float32)
    lead = None
    for (flip, p) in pieces:
        a = ((p.astype(jnp.float32) - row_mean[:, None]) / scale).astype(jnp.bfloat16)
        if lead is None:
            lead = jnp.concatenate([a, innovation], axis=1)
        part = lax.dot_general(lead, a, contract, preferred_element_type=jnp.float32)
        x = lax.dynamic_update_slice_in_dim(x, part, (e ^ flip) * group_size, axis=1)
    x = reduce_scatter(reduce_scatter(x, "y"), "x")
    parts = gather(x, "zl")
    x = ((parts[0] + parts[1]) + parts[2]) + parts[3]
    x = gather(gather(gather(x, "ens"), "x"), "y")
    x = jnp.moveaxis(x, 2, 0).reshape(ens_size, 2, group_size, members)
    gram_sum = x[:, 0].reshape(members, members)
    cross = x[:, 1].reshape(members, members).T
    gram = gram_sum + jnp.eye(members, dtype=jnp.float32)
    factor_inv = factor_inverse(gram)
    coef_partner, factor_inv = lax.optimization_barrier((coef_partner, factor_inv))
    weights = dot(factor_inv.T, dot(factor_inv, cross))
    coef_far = lax.ppermute(coef_partner, "ens", [(i, i ^ 1) for i in range(ens_size)])
    coef_blocks = jnp.stack([coef_own, coef_partner, coef_core, coef_far])
    coef_mean = jnp.mean(coef_blocks, axis=2, keepdims=True)
    coef_anomaly = (coef_blocks - coef_mean) / (members - 1) ** 0.5
    own_update = coef_blocks[:1] + jnp.einsum(
        "krm,mn->krn", coef_anomaly[:1], weights, precision=lax.Precision.HIGH
    )
    other_update = coef_blocks[1:] + jnp.einsum(
        "krm,mn->krn", coef_anomaly[1:], weights, preferred_element_type=jnp.float32
    )
    updated_blocks = jnp.concatenate([own_update, other_update])
    coef_low = jnp.take(
        updated_blocks.astype(jnp.bfloat16), jnp.array([0, 2, 1, 3])[jnp.arange(ens_size) ^ e], axis=0
    ).reshape(-1, members)
    rebuilt = lax.dot_general(
        coef_low, basis, (((0,), (0,)), ((), ())), preferred_element_type=jnp.float32
    )
    field = (mean_field[None, :] + rebuilt).astype(jnp.bfloat16)
    updated = updated_blocks[0]
    return (updated, field)


def solution(mesh):
    obs_size, ens_size = mesh.devices.shape
    side = round(obs_size ** (1 / 3))
    fine = Mesh(mesh.devices.reshape(side, side, obs_size // side**2, ens_size), (*OBS_AXES, "ens"))
    obs = OBS_AXES
    in_specs = (
        P(obs, "ens"),
        P(obs, "ens"),
        P(obs),
        P(obs),
        P("ens", None),
        P(None, (*obs, "ens")),
        P((*obs, "ens")),
    )
    out_specs = (P("ens", None), P(None, (*obs, "ens")))
    return jax.shard_map(shards, mesh=fine, in_specs=in_specs, out_specs=out_specs, check_vma=False)
```

```python
import jax
import jax.numpy as jnp
from jax import lax
from jax.sharding import Mesh
from jax.sharding import PartitionSpec as P


ALPHA = 4
OBS_AXES = ("y", "x", "zl")


def reduce_scatter(x, a):
    n = lax.axis_size(a)
    idx = lax.axis_index(a)
    chunks = x.reshape(n, x.shape[0] // n, *x.shape[1:])
    acc = lax.dynamic_index_in_dim(chunks, idx, 0, keepdims=False)
    for s in range(1, n):
        send = lax.dynamic_index_in_dim(chunks, (idx + s) % n, 0, keepdims=False)
        acc = acc + lax.ppermute(send, a, [(i, (i + s) % n) for i in range(n)])
    return acc


def gather(x, a):
    n = lax.axis_size(a)
    idx = lax.axis_index(a)
    parts = [x] + [lax.ppermute(x, a, [(i, (i - s) % n) for i in range(n)]) for s in range(1, n)]
    return jnp.roll(jnp.stack(parts), idx, axis=0)


def dot(a, b):
    return jnp.dot(a, b, precision=lax.Precision.HIGH)


def factor_inverse(m, base=128):
    n = m.shape[0]
    if n <= base:
        low = jnp.linalg.cholesky(m)
        return jax.scipy.linalg.solve_triangular(low, jnp.eye(n, dtype=m.dtype), lower=True)
    h = n // 2
    top_inv = factor_inverse(m[:h, :h], base)
    left = dot(m[h:, :h], top_inv.T)
    bottom_inv = factor_inverse(m[h:, h:] - dot(left, left.T), base)
    corner = -dot(bottom_inv, dot(left, top_inv))
    upper = jnp.concatenate([top_inv, jnp.zeros((h, n - h), m.dtype)], axis=1)
    lower = jnp.concatenate([corner, bottom_inv], axis=1)
    return jnp.concatenate([upper, lower], axis=0)


def shards(predicted, noise, observed, obs_error, coefficients, basis, mean_field):
    _, group_size = predicted.shape
    ens_size = lax.axis_size("ens")
    members = group_size * ens_size
    spread = ALPHA**0.5 * obs_error
    innovation = (
        (observed[:, None] - predicted.astype(jnp.float32)) / spread[:, None]
        + noise.astype(jnp.float32)
    ).astype(jnp.bfloat16)
    row_sum = predicted.astype(jnp.float32).sum(axis=1)
    row_sum = row_sum + lax.ppermute(row_sum, "ens", [(i, i ^ 2) for i in range(ens_size)])
    row_sum = row_sum + lax.ppermute(row_sum, "ens", [(i, i ^ 1) for i in range(ens_size)])
    row_mean = row_sum / members
    e = lax.axis_index("ens")
    core = lax.ppermute(predicted, "ens", [(i, i ^ 1) for i in range(ens_size)])
    partner = lax.ppermute(predicted, "ens", [(i, i ^ 2) for i in range(ens_size)])
    coef_own, partner = lax.optimization_barrier((coefficients, partner))
    coef_partner = lax.ppermute(coef_own, "ens", [(i, i ^ 2) for i in range(ens_size)])
    coef_core = lax.ppermute(coefficients, "ens", [(i, i ^ 1) for i in range(ens_size)])
    far = lax.ppermute(partner, "ens", [(i, i ^ 1) for i in range(ens_size)])
    pieces = [(0, predicted), (1, core), (2, partner), (3, far)]
    scale = (members - 1) ** 0.5 * spread[:, None]
    contract = (((0,), (0,)), ((), ()))
    x = jnp.zeros((2 * group_size, members), jnp.float32)
    lead = None
    for (flip, p) in pieces:
        a = ((p.astype(jnp.float32) - row_mean[:, None]) / scale).astype(jnp.bfloat16)
        if lead is None:
            lead = jnp.concatenate([a, innovation], axis=1)
        part = lax.dot_general(lead, a, contract, preferred_element_type=jnp.float32)
        x = lax.dynamic_update_slice_in_dim(x, part, (e ^ flip) * group_size, axis=1)
    x = reduce_scatter(reduce_scatter(x, "y"), "x")
    parts = gather(x, "zl")
    x = ((parts[0] + parts[1]) + parts[2]) + parts[3]
    x = gather(gather(gather(x, "ens"), "x"), "y")
    x = jnp.moveaxis(x, 2, 0).reshape(ens_size, 2, group_size, members)
    gram_sum = x[:, 0].reshape(members, members)
    cross = x[:, 1].reshape(members, members).T
    gram = gram_sum + jnp.eye(members, dtype=jnp.float32)
    factor_inv = factor_inverse(gram)
    coef_partner, factor_inv = lax.optimization_barrier((coef_partner, factor_inv))
    weights = dot(factor_inv.T, dot(factor_inv, cross))
    coef_far = lax.ppermute(coef_partner, "ens", [(i, i ^ 1) for i in range(ens_size)])
    coef_blocks = jnp.stack([coef_own, coef_partner, coef_core, coef_far])
    coef_mean = jnp.mean(coef_blocks, axis=2, keepdims=True)
    coef_anomaly = (coef_blocks - coef_mean) / (members - 1) ** 0.5
    updated = coef_own + jnp.dot(coef_anomaly[0], weights, precision=lax.Precision.HIGH)
    updated_blocks = jnp.concatenate([updated[None], coef_blocks[1:] + jnp.einsum(
        "krm,mn->krn", coef_anomaly[1:], weights, precision=lax.Precision.HIGH
    )])
    coef_low = jnp.take(
        updated_blocks.astype(jnp.bfloat16), jnp.array([0, 2, 1, 3])[jnp.arange(ens_size) ^ e], axis=0
    ).reshape(-1, members)
    rebuilt = lax.dot_general(
        coef_low, basis, (((0,), (0,)), ((), ())), preferred_element_type=jnp.float32
    )
    field = (mean_field[None, :] + rebuilt).astype(jnp.bfloat16)
    return (updated, field)


def solution(mesh):
    obs_size, ens_size = mesh.devices.shape
    side = round(obs_size ** (1 / 3))
    fine = Mesh(mesh.devices.reshape(side, side, obs_size // side**2, ens_size), (*OBS_AXES, "ens"))
    obs = OBS_AXES
    in_specs = (
        P(obs, "ens"),
        P(obs, "ens"),
        P(obs),
        P(obs),
        P("ens", None),
        P(None, (*obs, "ens")),
        P((*obs, "ens")),
    )
    out_specs = (P("ens", None), P(None, (*obs, "ens")))
    return jax.shard_map(shards, mesh=fine, in_specs=in_specs, out_specs=out_specs, check_vma=False)
```
